128 devices in a mesh: row: 8 (over x, core), col: 16 (over y, z).
Axes of the slice: x: 4, y: 4, z: 4, core: 2. Of those that a mesh axis runs over, the one named last changes fastest.
Arguments:
- density_values: bfloat16 [512, 8, 128, 128], P(('row', 'col')), may hold values from -0.59765625 to 0.59765625
- density_cols: int32 [512, 8], P(('row', 'col')), may hold values from -4 to 4, as said below
- density_counts: int32 [512], P(('row', 'col')), may hold values from 1 to 8, 3072 in all
- square_cols: int32 [512, 16], P(('row', 'col')), may hold values from -8 to 8, as said below
- update_cols: int32 [512, 16], P(('row', 'col')), may hold values from -12 to 12, as said below
- target_trace: float32 [1], replicated, may hold values from -8388608 to -1048576
Outputs:
- square: bfloat16 [512, 16, 128, 128], P(('row', 'col'))
- purified: bfloat16 [512, 16, 128, 128], P(('row', 'col'))
The draws below stay inside these ranges and needn't reach their ends.
Inputs may be any that keep to these rules, and one draw needn't show every extreme that they name: `density_cols`: distinct within a block row; every even block row holds -4, every odd one 4. `density_counts`: the live blocks of a row are its first slots. `square_cols`: distinct within a block row; every even block row holds -8, every odd one 2 * 4. `update_cols`: distinct within a block row; every even block row holds -12, every odd one 3 * 4.
All inputs are finite; a program needn't handle non-finite values.
Results may differ from the reference program's by a relative error of at most 0.0058.
Values may be sent and summed in bfloat16 or wider, within the bound.
No kernel may reach another device: no remote copies, remote signals or barrier semaphores. Data moves between devices by JAX's collectives and lax.ppermute only.
A program may use at most 192 MiB of HBM per device.

```python
import math
import jax
import jax.numpy as jnp
import numpy as np
from jax import lax

BLOCK = 128
NBLOCKS = 512
HALF = 4
DENSITY_SLOTS = 8
SQUARE_SLOTS = 16
UPDATE_SLOTS = 16


def choose_offsets(key, count_rows, half_span, keep_count):
    width_all = 2 * half_span + 1
    scores = jax.random.randint(key, (count_rows, width_all), 0, 1 << 20) * width_all
    scores = scores + jnp.arange(width_all, dtype=jnp.int32)[None, :]
    parity = jnp.arange(count_rows, dtype=jnp.int32) % 2
    places = jnp.arange(width_all, dtype=jnp.int32)[None, :]
    edge_mark = jnp.where(parity[:, None] == 0, places == 0, places == width_all - 1)
    scores = scores + edge_mark.astype(jnp.int32) * (1 << 26)
    ordering = jnp.argsort(-scores, axis=1)
    return (ordering[:, :keep_count] - half_span).astype(jnp.int32)


def draw_density_cols(key, part):
    return choose_offsets(jax.random.fold_in(key, 11), NBLOCKS, HALF, DENSITY_SLOTS)


def draw_square_cols(key, part):
    return choose_offsets(jax.random.fold_in(key, 23), NBLOCKS, 2 * HALF, SQUARE_SLOTS)


def draw_update_cols(key, part):
    return choose_offsets(jax.random.fold_in(key, 37), NBLOCKS, 3 * HALF, UPDATE_SLOTS)


def levels(stream_key, dims, shards, smallest, top_value):
    factor_of, own = 1.0, jax.random.fold_in(stream_key, 6)
    for dim, blocks in shards:
        heights = jnp.exp(jax.random.uniform(jax.random.fold_in(own, dim), (blocks,), jnp.float32, smallest / len(shards), top_value / len(shards)))
        factor_of = factor_of * jnp.repeat(heights, dims[dim] // blocks).reshape([-1 if axis == dim else 1 for axis in range(len(dims))])
    return factor_of


def split_up(number_of, total, most, slope):
    weights = [(1 << 20) // math.isqrt(grade ** slope) + 1 for grade in range(2, number_of + 1)]
    spare, holding = total - most - (number_of - 1), [1] * (number_of - 1)
    while spare > 0:
        candidates = [i for i in range(number_of - 1) if holding[i] < most]
        whole, left = sum([weights[i] for i in candidates]), spare
        for i in candidates:
            addition = min(most - holding[i], max(1, left * weights[i] // whole), spare)
            holding[i] = holding[i] + addition
            spare = spare - addition
    return np.array([most] + holding)


def uneven_parts(own_key, count, total, bound, lean):
    if count == 2:
        one = jax.random.randint(own_key, (), max(1, total - bound), min(bound, total - 1) + 1)
        return jnp.stack([one, total - one])
    sizes = jnp.asarray(split_up(count, total, bound, lean), jnp.int32)
    couples = (count - 1) // 2
    donor, receiver = sizes[1:1 + 2 * couples:2], sizes[2:2 + 2 * couples:2]
    room = jnp.minimum(donor - 1, bound - receiver)
    moved = jax.random.randint(jax.random.fold_in(own_key, 1), (couples,), 0, 1 << 20) % (room + 1)
    sizes = sizes.at[1:1 + 2 * couples:2].set(donor - moved).at[2:2 + 2 * couples:2].set(receiver + moved)
    return sizes[jax.random.permutation(jax.random.fold_in(own_key, 2), count)]


def scatter_about(key, dims, spread, bound, shards=(), held_as=jnp.bfloat16):
    values = jax.random.normal(key, dims, jnp.float32) * spread
    if len(shards) > 0:
        values = levels(key, dims, shards, -0.22, 0.18) * values
    return jnp.clip(values, min=-bound, max=bound).astype(held_as)


def setup_inputs(seed: int = 0) -> dict:
    keys = jax.random.split(jax.random.key(seed), 7)
    return {
        "density_values": scatter_about(keys[0], (NBLOCKS, DENSITY_SLOTS, BLOCK, BLOCK), 0.1, 0.59765625, ((0, 128),)),
        "density_cols": draw_density_cols(jax.random.fold_in(keys[6], 71), 0),
        "density_counts": uneven_parts(keys[2], NBLOCKS, NBLOCKS * DENSITY_SLOTS * 3 // 4, DENSITY_SLOTS, 2).astype(jnp.int32),
        "square_cols": draw_square_cols(jax.random.fold_in(keys[6], 71), 0),
        "update_cols": draw_update_cols(jax.random.fold_in(keys[6], 71), 0),
        "target_trace": jnp.clip(jax.random.uniform(keys[5], (1,), jnp.float32, -8388608, -1048576), -8388608, -1048576),
    }


def pair_product(left_blocks, left_cols, right_blocks, right_cols, anchor, result_cols):
    def one_row(position):
        sources = anchor + position + left_cols[position]
        picked = jnp.take(right_blocks, sources, axis=0).astype(jnp.float32)
        picked_cols = jnp.take(right_cols, sources, axis=0)
        reached = left_cols[position][:, None] + picked_cols
        matches = (result_cols[position][:, None, None] == reached[None, :, :]).astype(jnp.float32)
        chosen = jnp.einsum("tsp,spyz->tsyz", matches, picked).astype(jnp.bfloat16)
        chosen = lax.optimization_barrier(chosen)
        return jnp.einsum("sxy,tsyz->txz", left_blocks[position].astype(jnp.float32), chosen.astype(jnp.float32))
    return lax.map(one_row, jnp.arange(left_blocks.shape[0], dtype=jnp.int32))


def wrapped(values_in, margin_rows):
    return jnp.concatenate([values_in[-margin_rows:], values_in, values_in[:margin_rows]], axis=0)


def reference(density_values, density_cols, density_counts, square_cols, update_cols, target_trace):
    is_live = jnp.arange(DENSITY_SLOTS, dtype=jnp.int32)[None, :] < density_counts[:, None]
    masked = jnp.where(is_live[:, :, None, None], density_values, jnp.zeros_like(density_values))
    margin_rows = 2 * HALF
    masked_wide = wrapped(masked, margin_rows)
    cols_wide = wrapped(density_cols, margin_rows)
    square = pair_product(masked, density_cols, masked_wide, cols_wide, margin_rows, square_cols).astype(jnp.bfloat16)
    square_wide = wrapped(square, margin_rows)
    square_cols_wide = wrapped(square_cols, margin_rows)
    cube_part = pair_product(square, square_cols, masked_wide, cols_wide, margin_rows, update_cols)
    quartic_part = pair_product(square, square_cols, square_wide, square_cols_wide, margin_rows, update_cols)
    masked_float = masked.astype(jnp.float32)
    square_float = square.astype(jnp.float32)
    trace_two = jnp.sum(masked_float * masked_float)
    matching = (square_cols[:, :, None] == density_cols[:, None, :]).astype(jnp.float32)
    aligned = jnp.einsum("rts,rsxy->rtxy", matching, masked_float)
    trace_three = jnp.sum(square_float * aligned)
    trace_four = jnp.sum(square_float * square_float)
    gamma_mix = (target_trace[0] - 4.0 * trace_three + 3.0 * trace_four) / (trace_two - 2.0 * trace_three + trace_four + 1e-6)
    carry_mask = (update_cols[:, :, None] == square_cols[:, None, :]).astype(jnp.float32)
    carried = jnp.einsum("rtu,ruxy->rtxy", carry_mask, square_float)
    purified = ((4.0 - 2.0 * gamma_mix) * cube_part + (gamma_mix - 3.0) * quartic_part + gamma_mix * carried).astype(jnp.bfloat16)
    return square, purified
```

```python
import jax
import jax.numpy as jnp
from jax import lax
from jax.sharding import PartitionSpec as P

HALF = 4
BF16 = jnp.bfloat16
F32 = jnp.float32


def passed_along(value, axis, steps):
    count = lax.axis_size(axis)
    pairs = [(source, (source + steps) % count) for source in range(count)]
    return lax.ppermute(value, axis, pairs)


def assemble(earlier, own_parts, later):
    joined = []
    for member in range(len(own_parts)):
        pieces = (
            [arrival[member] for arrival in reversed(earlier)]
            + [own_parts[member]]
            + [arrival[member] for arrival in later]
        )
        joined.append(jnp.concatenate(pieces, axis=0))
    return tuple(joined)


def spread(blocks, columns, reach_devices):
    earlier, later = ([], [])
    for distance in range(1, reach_devices + 1):
        for heading in (1, -1):
            arrived = passed_along((blocks, columns), ("row", "col"), heading * distance)
            (earlier if heading == 1 else later).append(arrived)
    return assemble(earlier, (blocks, columns), later)


def place_onehot(first_row, row_count, columns, low, width):
    rows = jnp.arange(row_count, dtype=jnp.int32)[:, None, None] + first_row
    target = rows + columns[:, None, :] - low
    places = jnp.arange(width, dtype=jnp.int32)[None, :, None]
    return (target == places).astype(BF16)


def densify(blocks, columns, first_row, low, width):
    onehot = place_onehot(first_row, blocks.shape[0], columns, low, width)
    dense = jnp.einsum("rcs,rsyz->rycz", onehot, blocks, preferred_element_type=F32)
    return dense.astype(BF16)


def slab_matmul(left, right):
    r, b, k, _ = left.shape
    n = right.shape[2]
    out = jnp.dot(
        left.reshape(r * b, k * b), right.reshape(k * b, n * b), preferred_element_type=F32
    )
    return out.reshape(r, b, n, b)


def extract(dense, columns, low):
    onehot = place_onehot(0, dense.shape[0], columns, low, dense.shape[2])
    picked = jnp.einsum("rcs,rxcz->rsxz", onehot, dense, preferred_element_type=F32)
    return picked.astype(BF16)


def shards(density_values, density_cols, density_counts, square_cols, update_cols, target_trace):
    rows_here = density_values.shape[0]
    reach_devices = (2 * HALF + rows_here - 1) // rows_here
    margin = reach_devices * rows_here
    is_live = (
        jnp.arange(density_values.shape[1], dtype=jnp.int32)[None, :] < density_counts[:, None]
    )
    masked = jnp.where(is_live[:, :, None, None], density_values, jnp.zeros_like(density_values))
    masked_wide, cols_wide = spread(masked, density_cols, reach_devices)

    d_local = densify(masked, density_cols, 0, -HALF, rows_here + 2 * HALF)
    near = slice(margin - HALF, margin + rows_here + HALF)
    d_near = densify(masked_wide[near], cols_wide[near], -HALF, -2 * HALF, rows_here + 4 * HALF)
    square_dense = slab_matmul(d_local, d_near).astype(BF16)
    pattern = jnp.max(place_onehot(0, rows_here, square_cols, -2 * HALF, rows_here + 4 * HALF), axis=2)
    s_local = jnp.where(pattern[:, None, :, None] > 0, square_dense, jnp.zeros_like(square_dense))
    square = extract(s_local, square_cols, -2 * HALF)

    square_wide, square_cols_wide = spread(square, square_cols, reach_devices)
    far = slice(margin - 2 * HALF, margin + rows_here + 2 * HALF)
    d_far = densify(masked_wide[far], cols_wide[far], -2 * HALF, -3 * HALF, rows_here + 6 * HALF)
    s_far = densify(
        square_wide[far], square_cols_wide[far], -2 * HALF, -3 * HALF, rows_here + 6 * HALF
    )

    trace_two = jnp.sum(jnp.square(masked.astype(F32)))
    trace_three = jnp.sum(
        s_local[:, :, HALF : HALF + rows_here + 2 * HALF, :].astype(F32) * d_local.astype(F32)
    )
    trace_four = jnp.sum(jnp.square(s_local.astype(F32)))
    sums = lax.psum(jnp.stack([trace_two, trace_three, trace_four]), ("row", "col"))
    total_two, total_three, total_four = sums[0], sums[1], sums[2]

    cube_dense = slab_matmul(s_local, d_far)
    quartic_dense = slab_matmul(s_local, s_far)
    gamma_mix = (target_trace[0] - 4.0 * total_three + 3.0 * total_four) / (
        total_two - 2.0 * total_three + total_four + 1e-06
    )
    carried = jnp.pad(s_local, ((0, 0), (0, 0), (HALF, HALF), (0, 0))).astype(F32)
    purified_dense = (
        (4.0 - 2.0 * gamma_mix) * cube_dense
        + (gamma_mix - 3.0) * quartic_dense
        + gamma_mix * carried
    ).astype(BF16)
    purified = extract(purified_dense, update_cols, -3 * HALF)
    return (square, purified)


def solution(mesh):
    return jax.shard_map(
        shards,
        mesh=mesh,
        in_specs=(
            P(("row", "col"), None, None, None),
            P(("row", "col"), None),
            P(("row", "col")),
            P(("row", "col"), None),
            P(("row", "col"), None),
            P(),
        ),
        out_specs=(P(("row", "col"), None, None, None), P(("row", "col"), None, None, None)),
        check_vma=False,
    )
```

```python
import jax
import jax.numpy as jnp
from jax import lax
from jax.sharding import PartitionSpec as P

HALF = 4
BF16 = jnp.bfloat16
F32 = jnp.float32


def passed_along(value, axis, steps):
    count = lax.axis_size(axis)
    pairs = [(source, (source + steps) % count) for source in range(count)]
    return lax.ppermute(value, axis, pairs)


def assemble(earlier, own_parts, later):
    joined = []
    for member in range(len(own_parts)):
        pieces = (
            [arrival[member] for arrival in reversed(earlier)]
            + [own_parts[member]]
            + [arrival[member] for arrival in later]
        )
        joined.append(jnp.concatenate(pieces, axis=0))
    return tuple(joined)


def spread(blocks, columns, reach_devices):
    earlier, later = ([], [])
    for distance in range(1, reach_devices + 1):
        for heading in (1, -1):
            arrived = passed_along((blocks, columns), ("row", "col"), heading * distance)
            (earlier if heading == 1 else later).append(arrived)
    return assemble(earlier, (blocks, columns), later)


def butterfly_sum(value, axes):
    count = 1
    for axis in axes:
        count *= lax.axis_size(axis)
    step = 1
    while step < count:
        pairs = [(source, source ^ step) for source in range(count)]
        value = value + lax.ppermute(value, axes, pairs)
        step *= 2
    return value


def place_onehot(first_row, row_count, columns, low, width):
    rows = jnp.arange(row_count, dtype=jnp.int32)[:, None, None] + first_row
    target = rows + columns[:, None, :] - low
    places = jnp.arange(width, dtype=jnp.int32)[None, :, None]
    return (target == places).astype(BF16)


def densify(blocks, columns, first_row, low, width):
    onehot = place_onehot(first_row, blocks.shape[0], columns, low, width)
    dense = jnp.einsum("rcs,rsyz->rycz", onehot, blocks, preferred_element_type=F32)
    return dense.astype(BF16)


def slab_matmul(left, right):
    r, b, k, _ = left.shape
    n = right.shape[2]
    out = jnp.dot(
        left.reshape(r * b, k * b), right.reshape(k * b, n * b), preferred_element_type=F32
    )
    return out.reshape(r, b, n, b)


def extract(dense, columns, low):
    onehot = place_onehot(0, dense.shape[0], columns, low, dense.shape[2])
    picked = jnp.einsum("rcs,rxcz->rsxz", onehot, dense, preferred_element_type=F32)
    return picked.astype(BF16)


def shards(density_values, density_cols, density_counts, square_cols, update_cols, target_trace):
    rows_here = density_values.shape[0]
    reach_devices = (2 * HALF + rows_here - 1) // rows_here
    margin = reach_devices * rows_here
    is_live = (
        jnp.arange(density_values.shape[1], dtype=jnp.int32)[None, :] < density_counts[:, None]
    )
    masked = jnp.where(is_live[:, :, None, None], density_values, jnp.zeros_like(density_values))
    masked_wide, cols_wide = spread(masked, density_cols, reach_devices)

    d_local = densify(masked, density_cols, 0, -HALF, rows_here + 2 * HALF)
    near = slice(margin - HALF, margin + rows_here + HALF)
    d_near = densify(masked_wide[near], cols_wide[near], -HALF, -2 * HALF, rows_here + 4 * HALF)
    square_dense = slab_matmul(d_local, d_near).astype(BF16)
    pattern = jnp.max(place_onehot(0, rows_here, square_cols, -2 * HALF, rows_here + 4 * HALF), axis=2)
    s_local = jnp.where(pattern[:, None, :, None] > 0, square_dense, jnp.zeros_like(square_dense))
    square = extract(s_local, square_cols, -2 * HALF)

    square_wide, square_cols_wide = spread(square, square_cols, reach_devices)
    far = slice(margin - 2 * HALF, margin + rows_here + 2 * HALF)
    d_far = densify(masked_wide[far], cols_wide[far], -2 * HALF, -3 * HALF, rows_here + 6 * HALF)
    s_far = densify(
        square_wide[far], square_cols_wide[far], -2 * HALF, -3 * HALF, rows_here + 6 * HALF
    )

    trace_two = jnp.sum(jnp.square(masked.astype(F32)))
    trace_three = jnp.sum(
        s_local[:, :, HALF : HALF + rows_here + 2 * HALF, :].astype(F32) * d_local.astype(F32)
    )
    trace_four = jnp.sum(jnp.square(s_local.astype(F32)))
    sums = butterfly_sum(jnp.stack([trace_two, trace_three, trace_four]), ("row", "col"))
    total_two, total_three, total_four = sums[0], sums[1], sums[2]

    cube_dense = slab_matmul(s_local, d_far)
    quartic_dense = slab_matmul(s_local, s_far)
    gamma_mix = (target_trace[0] - 4.0 * total_three + 3.0 * total_four) / (
        total_two - 2.0 * total_three + total_four + 1e-06
    )
    carried = jnp.pad(s_local, ((0, 0), (0, 0), (HALF, HALF), (0, 0))).astype(F32)
    purified_dense = (
        (4.0 - 2.0 * gamma_mix) * cube_dense
        + (gamma_mix - 3.0) * quartic_dense
        + gamma_mix * carried
    ).astype(BF16)
    purified = extract(purified_dense, update_cols, -3 * HALF)
    return (square, purified)


def solution(mesh):
    return jax.shard_map(
        shards,
        mesh=mesh,
        in_specs=(
            P(("row", "col"), None, None, None),
            P(("row", "col"), None),
            P(("row", "col")),
            P(("row", "col"), None),
            P(("row", "col"), None),
            P(),
        ),
        out_specs=(P(("row", "col"), None, None, None), P(("row", "col"), None, None, None)),
        check_vma=False,
    )
```

```python
import jax
import jax.numpy as jnp
from jax import lax
from jax.sharding import PartitionSpec as P

HALF = 4
BF16 = jnp.bfloat16
F32 = jnp.float32


def passed_along(value, axis, steps):
    count = lax.axis_size(axis)
    pairs = [(source, (source + steps) % count) for source in range(count)]
    return lax.ppermute(value, axis, pairs)


def assemble(earlier, own_parts, later):
    joined = []
    for member in range(len(own_parts)):
        pieces = (
            [arrival[member] for arrival in reversed(earlier)]
            + [own_parts[member]]
            + [arrival[member] for arrival in later]
        )
        joined.append(jnp.concatenate(pieces, axis=0))
    return tuple(joined)


def spread(blocks, columns, reach_devices):
    earlier, later = ([], [])
    for heading, arrivals in ((1, earlier), (-1, later)):
        carried = (blocks, columns)
        for _ in range(reach_devices):
            carried = passed_along(carried, ("row", "col"), heading)
            arrivals.append(carried)
    return assemble(earlier, (blocks, columns), later)


def butterfly_sum(value, axes):
    count = 1
    for axis in axes:
        count *= lax.axis_size(axis)
    step = 1
    while step < count:
        pairs = [(source, source ^ step) for source in range(count)]
        value = value + lax.ppermute(value, axes, pairs)
        step *= 2
    return value


def place_onehot(first_row, row_count, columns, low, width):
    rows = jnp.arange(row_count, dtype=jnp.int32)[:, None, None] + first_row
    target = rows + columns[:, None, :] - low
    places = jnp.arange(width, dtype=jnp.int32)[None, :, None]
    return (target == places).astype(BF16)


def densify(blocks, columns, first_row, low, width):
    onehot = place_onehot(first_row, blocks.shape[0], columns, low, width)
    dense = jnp.einsum("rcs,rsyz->rycz", onehot, blocks, preferred_element_type=F32)
    return dense.astype(BF16)


def slab_matmul(left, right):
    r, b, k, _ = left.shape
    n = right.shape[2]
    out = jnp.dot(
        left.reshape(r * b, k * b), right.reshape(k * b, n * b), preferred_element_type=F32
    )
    return out.reshape(r, b, n, b)


def extract(dense, columns, low):
    onehot = place_onehot(0, dense.shape[0], columns, low, dense.shape[2])
    picked = jnp.einsum("rcs,rxcz->rsxz", onehot, dense, preferred_element_type=F32)
    return picked.astype(BF16)


def shards(density_values, density_cols, density_counts, square_cols, update_cols, target_trace):
    rows_here = density_values.shape[0]
    reach_devices = (2 * HALF + rows_here - 1) // rows_here
    margin = reach_devices * rows_here
    is_live = (
        jnp.arange(density_values.shape[1], dtype=jnp.int32)[None, :] < density_counts[:, None]
    )
    masked = jnp.where(is_live[:, :, None, None], density_values, jnp.zeros_like(density_values))
    masked_wide, cols_wide = spread(masked, density_cols, reach_devices)

    d_local = densify(masked, density_cols, 0, -HALF, rows_here + 2 * HALF)
    near = slice(margin - HALF, margin + rows_here + HALF)
    d_near = densify(masked_wide[near], cols_wide[near], -HALF, -2 * HALF, rows_here + 4 * HALF)
    square_dense = slab_matmul(d_local, d_near).astype(BF16)
    pattern = jnp.max(place_onehot(0, rows_here, square_cols, -2 * HALF, rows_here + 4 * HALF), axis=2)
    s_local = jnp.where(pattern[:, None, :, None] > 0, square_dense, jnp.zeros_like(square_dense))
    square = extract(s_local, square_cols, -2 * HALF)

    square_wide, square_cols_wide = spread(square, square_cols, reach_devices)
    far = slice(margin - 2 * HALF, margin + rows_here + 2 * HALF)
    d_far = densify(masked_wide[far], cols_wide[far], -2 * HALF, -3 * HALF, rows_here + 6 * HALF)
    s_far = densify(
        square_wide[far], square_cols_wide[far], -2 * HALF, -3 * HALF, rows_here + 6 * HALF
    )

    trace_two = jnp.sum(jnp.square(masked.astype(F32)))
    trace_three = jnp.sum(
        s_local[:, :, HALF : HALF + rows_here + 2 * HALF, :].astype(F32) * d_local.astype(F32)
    )
    trace_four = jnp.sum(jnp.square(s_local.astype(F32)))
    local_sums, _ = lax.optimization_barrier(
        (jnp.stack([trace_two, trace_three, trace_four]), square_wide)
    )
    sums = butterfly_sum(local_sums, ("row", "col"))
    total_two, total_three, total_four = sums[0], sums[1], sums[2]

    cube_dense = slab_matmul(s_local, d_far)
    quartic_dense = slab_matmul(s_local, s_far)
    gamma_mix = (target_trace[0] - 4.0 * total_three + 3.0 * total_four) / (
        total_two - 2.0 * total_three + total_four + 1e-06
    )
    carried = jnp.pad(s_local, ((0, 0), (0, 0), (HALF, HALF), (0, 0))).astype(F32)
    purified_dense = (
        (4.0 - 2.0 * gamma_mix) * cube_dense
        + (gamma_mix - 3.0) * quartic_dense
        + gamma_mix * carried
    ).astype(BF16)
    purified = extract(purified_dense, update_cols, -3 * HALF)
    return (square, purified)


def solution(mesh):
    return jax.shard_map(
        shards,
        mesh=mesh,
        in_specs=(
            P(("row", "col"), None, None, None),
            P(("row", "col"), None),
            P(("row", "col")),
            P(("row", "col"), None),
            P(("row", "col"), None),
            P(),
        ),
        out_specs=(P(("row", "col"), None, None, None), P(("row", "col"), None, None, None)),
        check_vma=False,
    )
```

```python
import jax
import jax.numpy as jnp
from jax import lax
from jax.experimental import pallas as pl
from jax.experimental.pallas import tpu as pltpu
from jax.sharding import PartitionSpec as P

HALF = 4
BF16 = jnp.bfloat16
F32 = jnp.float32


def passed_along(value, axis, steps):
    count = lax.axis_size(axis)
    pairs = [(source, (source + steps) % count) for source in range(count)]
    return lax.ppermute(value, axis, pairs)


def assemble(earlier, own_parts, later):
    joined = []
    for member in range(len(own_parts)):
        pieces = (
            [arrival[member] for arrival in reversed(earlier)]
            + [own_parts[member]]
            + [arrival[member] for arrival in later]
        )
        joined.append(jnp.concatenate(pieces, axis=0))
    return tuple(joined)


def spread(blocks, columns, reach_devices):
    earlier, later = ([], [])
    for heading, arrivals in ((1, earlier), (-1, later)):
        carried = (blocks, columns)
        for _ in range(reach_devices):
            carried = passed_along(carried, ("row", "col"), heading)
            arrivals.append(carried)
    return assemble(earlier, (blocks, columns), later)


def butterfly_sum(value, axes):
    count = 1
    for axis in axes:
        count *= lax.axis_size(axis)
    step = 1
    while step < count:
        pairs = [(source, source ^ step) for source in range(count)]
        value = value + lax.ppermute(value, axes, pairs)
        step *= 2
    return value


def place_onehot(first_row, row_count, columns, low, width):
    rows = jnp.arange(row_count, dtype=jnp.int32)[:, None, None] + first_row
    target = rows + columns[:, None, :] - low
    places = jnp.arange(width, dtype=jnp.int32)[None, :, None]
    return (target == places).astype(BF16)


def densify(blocks, columns, first_row, low, width):
    onehot = place_onehot(first_row, blocks.shape[0], columns, low, width)
    dense = jnp.einsum("rcs,rsyz->rycz", onehot, blocks, preferred_element_type=F32)
    return dense.astype(BF16)


def densify_transposed(blocks, columns, first_row, low, width):
    count, slots, b, _ = blocks.shape
    rows = jnp.arange(count, dtype=jnp.int32)[:, None] + first_row
    place = rows + columns - low
    valid = ((place >= 0) & (place < width)).astype(jnp.int32)
    place = jnp.where(valid > 0, place, 0).astype(jnp.int32)

    def kernel(place_ref, valid_ref, blocks_ref, out_ref):
        def clear(c, carry):
            start = pl.multiple_of(c * b, b)
            out_ref[pl.ds(start, b), :] = jnp.zeros((b, count * b), out_ref.dtype)
            return carry

        lax.fori_loop(0, width, clear, 0)

        def put(i, carry):
            r = i // slots
            s = i % slots

            @pl.when(valid_ref[r, s] > 0)
            def _():
                top = pl.multiple_of(place_ref[r, s] * b, b)
                left = pl.multiple_of(r * b, b)
                block = blocks_ref[r, s].astype(F32).T.astype(out_ref.dtype)
                out_ref[pl.ds(top, b), pl.ds(left, b)] = block

            return carry

        lax.fori_loop(0, count * slots, put, 0)

    moved = blocks.size * 2 + width * b * count * b * 2
    return pl.pallas_call(
        kernel,
        out_shape=jax.ShapeDtypeStruct((width * b, count * b), BF16),
        in_specs=[
            pl.BlockSpec(memory_space=pltpu.SMEM),
            pl.BlockSpec(memory_space=pltpu.SMEM),
            pl.BlockSpec(memory_space=pltpu.VMEM),
        ],
        out_specs=pl.BlockSpec(memory_space=pltpu.VMEM),
        cost_estimate=pl.CostEstimate(flops=0, bytes_accessed=moved, transcendentals=0),
    )(place, valid, blocks)


def slab_matmul_nt(left, right_t):
    r, b, k, _ = left.shape
    n = right_t.shape[0] // b
    out = lax.dot_general(
        left.reshape(r * b, k * b), right_t, (((1,), (1,)), ((), ())), preferred_element_type=F32
    )
    return out.reshape(r, b, n, b)


def slab_matmul(left, right):
    r, b, k, _ = left.shape
    n = right.shape[2]
    out = jnp.dot(
        left.reshape(r * b, k * b), right.reshape(k * b, n * b), preferred_element_type=F32
    )
    return out.reshape(r, b, n, b)


def extract(dense, columns, low):
    onehot = place_onehot(0, dense.shape[0], columns, low, dense.shape[2])
    picked = jnp.einsum("rcs,rxcz->rsxz", onehot, dense, preferred_element_type=F32)
    return picked.astype(BF16)


def shards(density_values, density_cols, density_counts, square_cols, update_cols, target_trace):
    rows_here = density_values.shape[0]
    reach_devices = (2 * HALF + rows_here - 1) // rows_here
    margin = reach_devices * rows_here
    is_live = (
        jnp.arange(density_values.shape[1], dtype=jnp.int32)[None, :] < density_counts[:, None]
    )
    masked = jnp.where(is_live[:, :, None, None], density_values, jnp.zeros_like(density_values))
    masked_wide, cols_wide = spread(masked, density_cols, reach_devices)

    d_local = densify(masked, density_cols, 0, -HALF, rows_here + 2 * HALF)
    near = slice(margin - HALF, margin + rows_here + HALF)
    d_near = densify_transposed(
        masked_wide[near], cols_wide[near], -HALF, -2 * HALF, rows_here + 4 * HALF
    )
    square_dense = slab_matmul_nt(d_local, d_near).astype(BF16)
    pattern = jnp.max(place_onehot(0, rows_here, square_cols, -2 * HALF, rows_here + 4 * HALF), axis=2)
    s_local = jnp.where(pattern[:, None, :, None] > 0, square_dense, jnp.zeros_like(square_dense))
    square = extract(s_local, square_cols, -2 * HALF)

    square_wide, square_cols_wide = spread(square, square_cols, reach_devices)
    far = slice(margin - 2 * HALF, margin + rows_here + 2 * HALF)
    d_far = densify_transposed(
        masked_wide[far], cols_wide[far], -2 * HALF, -3 * HALF, rows_here + 6 * HALF
    )
    s_far = densify_transposed(
        square_wide[far], square_cols_wide[far], -2 * HALF, -3 * HALF, rows_here + 6 * HALF
    )

    trace_two = jnp.sum(jnp.square(masked.astype(F32)))
    trace_three = jnp.sum(
        s_local[:, :, HALF : HALF + rows_here + 2 * HALF, :].astype(F32) * d_local.astype(F32)
    )
    trace_four = jnp.sum(jnp.square(s_local.astype(F32)))
    local_sums, _ = lax.optimization_barrier(
        (jnp.stack([trace_two, trace_three, trace_four]), square_wide)
    )
    sums = butterfly_sum(local_sums, ("row", "col"))
    total_two, total_three, total_four = sums[0], sums[1], sums[2]

    cube_dense = slab_matmul_nt(s_local, d_far)
    quartic_dense = slab_matmul_nt(s_local, s_far)
    gamma_mix = (target_trace[0] - 4.0 * total_three + 3.0 * total_four) / (
        total_two - 2.0 * total_three + total_four + 1e-06
    )
    carried = jnp.pad(s_local, ((0, 0), (0, 0), (HALF, HALF), (0, 0))).astype(F32)
    purified_dense = (
        (4.0 - 2.0 * gamma_mix) * cube_dense
        + (gamma_mix - 3.0) * quartic_dense
        + gamma_mix * carried
    ).astype(BF16)
    purified = extract(purified_dense, update_cols, -3 * HALF)
    return (square, purified)


def solution(mesh):
    return jax.shard_map(
        shards,
        mesh=mesh,
        in_specs=(
            P(("row", "col"), None, None, None),
            P(("row", "col"), None),
            P(("row", "col")),
            P(("row", "col"), None),
            P(("row", "col"), None),
            P(),
        ),
        out_specs=(P(("row", "col"), None, None, None), P(("row", "col"), None, None, None)),
        check_vma=False,
    )
```

```python
import jax
import jax.numpy as jnp
from jax import lax
from jax.experimental import pallas as pl
from jax.experimental.pallas import tpu as pltpu
from jax.sharding import PartitionSpec as P

HALF = 4
BF16 = jnp.bfloat16
F32 = jnp.float32


def passed_along(value, axis, steps):
    count = lax.axis_size(axis)
    pairs = [(source, (source + steps) % count) for source in range(count)]
    return lax.ppermute(value, axis, pairs)


def assemble(earlier, own_parts, later):
    joined = []
    for member in range(len(own_parts)):
        pieces = (
            [arrival[member] for arrival in reversed(earlier)]
            + [own_parts[member]]
            + [arrival[member] for arrival in later]
        )
        joined.append(jnp.concatenate(pieces, axis=0))
    return tuple(joined)


def spread(blocks, columns, reach_devices):
    earlier, later = ([], [])
    for heading, arrivals in ((1, earlier), (-1, later)):
        carried = (blocks, columns)
        for _ in range(reach_devices):
            carried = passed_along(carried, ("row", "col"), heading)
            arrivals.append(carried)
    return assemble(earlier, (blocks, columns), later)


def butterfly_sum(value, axes):
    count = 1
    for axis in axes:
        count *= lax.axis_size(axis)
    step = 1
    while step < count:
        pairs = [(source, source ^ step) for source in range(count)]
        value = value + lax.ppermute(value, axes, pairs)
        step *= 2
    return value


def place_onehot(first_row, row_count, columns, low, width):
    rows = jnp.arange(row_count, dtype=jnp.int32)[:, None, None] + first_row
    target = rows + columns[:, None, :] - low
    places = jnp.arange(width, dtype=jnp.int32)[None, :, None]
    return (target == places).astype(BF16)


def densify(blocks, columns, first_row, low, width):
    onehot = place_onehot(first_row, blocks.shape[0], columns, low, width)
    dense = jnp.einsum("rcs,rsyz->rycz", onehot, blocks, preferred_element_type=F32)
    return dense.astype(BF16)


def densify_transposed(blocks, columns, first_row, low, width):
    count, slots, b, _ = blocks.shape
    rows = jnp.arange(count, dtype=jnp.int32)[:, None] + first_row
    place = rows + columns - low
    valid = ((place >= 0) & (place < width)).astype(jnp.int32)
    place = jnp.where(valid > 0, place, 0).astype(jnp.int32)

    def kernel(place_ref, valid_ref, blocks_ref, out_ref):
        def clear(c, carry):
            start = pl.multiple_of(c * b, b)
            out_ref[pl.ds(start, b), :] = jnp.zeros((b, count * b), out_ref.dtype)
            return carry

        lax.fori_loop(0, width, clear, 0)

        def put(i, carry):
            r = i // slots
            s = i % slots

            @pl.when(valid_ref[r, s] > 0)
            def _():
                top = pl.multiple_of(place_ref[r, s] * b, b)
                left = pl.multiple_of(r * b, b)
                out_ref[pl.ds(top, b), pl.ds(left, b)] = blocks_ref[r, s]

            return carry

        lax.fori_loop(0, count * slots, put, 0)

    moved = blocks.size * 2 + width * b * count * b * 2
    return pl.pallas_call(
        kernel,
        out_shape=jax.ShapeDtypeStruct((width * b, count * b), BF16),
        in_specs=[
            pl.BlockSpec(memory_space=pltpu.SMEM),
            pl.BlockSpec(memory_space=pltpu.SMEM),
            pl.BlockSpec(memory_space=pltpu.VMEM),
        ],
        out_specs=pl.BlockSpec(memory_space=pltpu.VMEM),
        cost_estimate=pl.CostEstimate(flops=0, bytes_accessed=moved, transcendentals=0),
    )(place, valid, blocks)


def slab_matmul_nt(left, right_t):
    r, b, k, _ = left.shape
    n = right_t.shape[0] // b
    out = lax.dot_general(
        left.reshape(r * b, k * b), right_t, (((1,), (1,)), ((), ())), preferred_element_type=F32
    )
    return out.reshape(r, b, n, b)


def slab_matmul(left, right):
    r, b, k, _ = left.shape
    n = right.shape[2]
    out = jnp.dot(
        left.reshape(r * b, k * b), right.reshape(k * b, n * b), preferred_element_type=F32
    )
    return out.reshape(r, b, n, b)


def extract(dense, columns, low):
    onehot = place_onehot(0, dense.shape[0], columns, low, dense.shape[2])
    picked = jnp.einsum("rcs,rxcz->rsxz", onehot, dense, preferred_element_type=F32)
    return picked.astype(BF16)


def shards(density_values, density_cols, density_counts, square_cols, update_cols, target_trace):
    rows_here = density_values.shape[0]
    reach_devices = (2 * HALF + rows_here - 1) // rows_here
    margin = reach_devices * rows_here
    is_live = (
        jnp.arange(density_values.shape[1], dtype=jnp.int32)[None, :] < density_counts[:, None]
    )
    masked = jnp.where(is_live[:, :, None, None], density_values, jnp.zeros_like(density_values))
    masked_wide, cols_wide = spread(jnp.swapaxes(masked, 2, 3), density_cols, reach_devices)

    d_local = densify(masked, density_cols, 0, -HALF, rows_here + 2 * HALF)
    near = slice(margin - HALF, margin + rows_here + HALF)
    d_near = densify_transposed(
        masked_wide[near], cols_wide[near], -HALF, -2 * HALF, rows_here + 4 * HALF
    )
    square_dense = slab_matmul_nt(d_local, d_near).astype(BF16)
    pattern = jnp.max(place_onehot(0, rows_here, square_cols, -2 * HALF, rows_here + 4 * HALF), axis=2)
    s_local = jnp.where(pattern[:, None, :, None] > 0, square_dense, jnp.zeros_like(square_dense))
    square = extract(s_local, square_cols, -2 * HALF)

    square_wide, square_cols_wide = spread(jnp.swapaxes(square, 2, 3), square_cols, reach_devices)
    far = slice(margin - 2 * HALF, margin + rows_here + 2 * HALF)
    d_far = densify_transposed(
        masked_wide[far], cols_wide[far], -2 * HALF, -3 * HALF, rows_here + 6 * HALF
    )
    s_far = densify_transposed(
        square_wide[far], square_cols_wide[far], -2 * HALF, -3 * HALF, rows_here + 6 * HALF
    )

    trace_two = jnp.sum(jnp.square(masked.astype(F32)))
    trace_three = jnp.sum(
        s_local[:, :, HALF : HALF + rows_here + 2 * HALF, :].astype(F32) * d_local.astype(F32)
    )
    trace_four = jnp.sum(jnp.square(s_local.astype(F32)))
    local_sums, _ = lax.optimization_barrier(
        (jnp.stack([trace_two, trace_three, trace_four]), square_wide)
    )
    sums = butterfly_sum(local_sums, ("row", "col"))
    total_two, total_three, total_four = sums[0], sums[1], sums[2]

    cube_dense = slab_matmul_nt(s_local, d_far)
    quartic_dense = slab_matmul_nt(s_local, s_far)
    gamma_mix = (target_trace[0] - 4.0 * total_three + 3.0 * total_four) / (
        total_two - 2.0 * total_three + total_four + 1e-06
    )
    carried = jnp.pad(s_local, ((0, 0), (0, 0), (HALF, HALF), (0, 0))).astype(F32)
    purified_dense = (
        (4.0 - 2.0 * gamma_mix) * cube_dense
        + (gamma_mix - 3.0) * quartic_dense
        + gamma_mix * carried
    ).astype(BF16)
    purified = extract(purified_dense, update_cols, -3 * HALF)
    return (square, purified)


def solution(mesh):
    return jax.shard_map(
        shards,
        mesh=mesh,
        in_specs=(
            P(("row", "col"), None, None, None),
            P(("row", "col"), None),
            P(("row", "col")),
            P(("row", "col"), None),
            P(("row", "col"), None),
            P(),
        ),
        out_specs=(P(("row", "col"), None, None, None), P(("row", "col"), None, None, None)),
        check_vma=False,
    )
```

```python
import jax
import jax.numpy as jnp
from jax import lax
from jax.experimental import pallas as pl
from jax.experimental.pallas import tpu as pltpu
from jax.sharding import PartitionSpec as P

HALF = 4
BF16 = jnp.bfloat16
F32 = jnp.float32


def passed_along(value, axis, steps):
    count = lax.axis_size(axis)
    pairs = [(source, (source + steps) % count) for source in range(count)]
    return lax.ppermute(value, axis, pairs)


def assemble(earlier, own_parts, later):
    joined = []
    for member in range(len(own_parts)):
        pieces = (
            [arrival[member] for arrival in reversed(earlier)]
            + [own_parts[member]]
            + [arrival[member] for arrival in later]
        )
        joined.append(jnp.concatenate(pieces, axis=0))
    return tuple(joined)


def spread(blocks, columns, reach_devices):
    earlier, later = ([], [])
    for heading, arrivals in ((1, earlier), (-1, later)):
        carried = (blocks, columns)
        for _ in range(reach_devices):
            carried = passed_along(carried, ("row", "col"), heading)
            arrivals.append(carried)
    return assemble(earlier, (blocks, columns), later)


def butterfly_sum(value, axes):
    count = 1
    for axis in axes:
        count *= lax.axis_size(axis)
    step = 1
    while step < count:
        pairs = [(source, source ^ step) for source in range(count)]
        value = value + lax.ppermute(value, axes, pairs)
        step *= 2
    return value


def place_onehot(first_row, row_count, columns, low, width):
    rows = jnp.arange(row_count, dtype=jnp.int32)[:, None, None] + first_row
    target = rows + columns[:, None, :] - low
    places = jnp.arange(width, dtype=jnp.int32)[None, :, None]
    return (target == places).astype(BF16)


def densify(blocks, columns, first_row, low, width):
    onehot = place_onehot(first_row, blocks.shape[0], columns, low, width)
    dense = jnp.einsum("rcs,rsyz->rycz", onehot, blocks, preferred_element_type=F32)
    return dense.astype(BF16)


def densify_transposed(blocks, columns, first_row, low, width):
    count, slots, b, _ = blocks.shape
    rows = jnp.arange(count, dtype=jnp.int32)[:, None] + first_row
    place = rows + columns - low
    valid = ((place >= 0) & (place < width)).astype(jnp.int32)
    place = jnp.where(valid > 0, place, 0).astype(jnp.int32)

    def kernel(place_ref, valid_ref, blocks_ref, out_ref):
        def clear(c, carry):
            start = pl.multiple_of(c * b, b)
            out_ref[pl.ds(start, b), :] = jnp.zeros((b, count * b), out_ref.dtype)
            return carry

        lax.fori_loop(0, width, clear, 0)

        def put(i, carry):
            r = i // slots
            s = i % slots

            @pl.when(valid_ref[r, s] > 0)
            def _():
                top = pl.multiple_of(place_ref[r, s] * b, b)
                left = pl.multiple_of(r * b, b)
                out_ref[pl.ds(top, b), pl.ds(left, b)] = blocks_ref[r, s]

            return carry

        lax.fori_loop(0, count * slots, put, 0)

    moved = blocks.size * 2 + width * b * count * b * 2
    return pl.pallas_call(
        kernel,
        out_shape=jax.ShapeDtypeStruct((width * b, count * b), BF16),
        in_specs=[
            pl.BlockSpec(memory_space=pltpu.SMEM),
            pl.BlockSpec(memory_space=pltpu.SMEM),
            pl.BlockSpec(memory_space=pltpu.VMEM),
        ],
        out_specs=pl.BlockSpec(memory_space=pltpu.VMEM),
        cost_estimate=pl.CostEstimate(flops=0, bytes_accessed=moved, transcendentals=0),
    )(place, valid, blocks)


def slab_matmul_nt(left, right_t):
    r, b, k, _ = left.shape
    n = right_t.shape[0] // b
    out = lax.dot_general(
        left.reshape(r * b, k * b), right_t, (((1,), (1,)), ((), ())), preferred_element_type=F32
    )
    return out.reshape(r, b, n, b)


def slab_matmul(left, right):
    r, b, k, _ = left.shape
    n = right.shape[2]
    out = jnp.dot(
        left.reshape(r * b, k * b), right.reshape(k * b, n * b), preferred_element_type=F32
    )
    return out.reshape(r, b, n, b)


def extract(dense, columns, low):
    onehot = place_onehot(0, dense.shape[0], columns, low, dense.shape[2])
    picked = jnp.einsum("rcs,rxcz->rsxz", onehot, dense, preferred_element_type=F32)
    return picked.astype(BF16)


def pick(dense, columns, low):
    places = jnp.arange(dense.shape[0], dtype=jnp.int32)[:, None] + columns - low
    picked = jnp.take_along_axis(dense, places[:, None, :, None], axis=2)
    return jnp.transpose(picked, (0, 2, 1, 3))


def shards(density_values, density_cols, density_counts, square_cols, update_cols, target_trace):
    rows_here = density_values.shape[0]
    reach_devices = (2 * HALF + rows_here - 1) // rows_here
    margin = reach_devices * rows_here
    is_live = (
        jnp.arange(density_values.shape[1], dtype=jnp.int32)[None, :] < density_counts[:, None]
    )
    masked = jnp.where(is_live[:, :, None, None], density_values, jnp.zeros_like(density_values))
    masked_wide, cols_wide = spread(jnp.swapaxes(masked, 2, 3), density_cols, reach_devices)

    d_local = densify(masked, density_cols, 0, -HALF, rows_here + 2 * HALF)
    near = slice(margin - HALF, margin + rows_here + HALF)
    d_near = densify_transposed(
        masked_wide[near], cols_wide[near], -HALF, -2 * HALF, rows_here + 4 * HALF
    )
    square_dense = slab_matmul_nt(d_local, d_near).astype(BF16)
    pattern = jnp.max(place_onehot(0, rows_here, square_cols, -2 * HALF, rows_here + 4 * HALF), axis=2)
    s_local = jnp.where(pattern[:, None, :, None] > 0, square_dense, jnp.zeros_like(square_dense))
    square = extract(s_local, square_cols, -2 * HALF)

    square_wide, square_cols_wide = spread(jnp.swapaxes(square, 2, 3), square_cols, reach_devices)
    far = slice(margin - 2 * HALF, margin + rows_here + 2 * HALF)
    d_far = densify_transposed(
        masked_wide[far], cols_wide[far], -2 * HALF, -3 * HALF, rows_here + 6 * HALF
    )
    s_far = densify_transposed(
        square_wide[far], square_cols_wide[far], -2 * HALF, -3 * HALF, rows_here + 6 * HALF
    )

    trace_two = jnp.sum(jnp.square(masked.astype(F32)))
    trace_three = jnp.sum(
        s_local[:, :, HALF : HALF + rows_here + 2 * HALF, :].astype(F32) * d_local.astype(F32)
    )
    trace_four = jnp.sum(jnp.square(s_local.astype(F32)))
    local_sums, _ = lax.optimization_barrier(
        (jnp.stack([trace_two, trace_three, trace_four]), square_wide)
    )
    sums = butterfly_sum(local_sums, ("row", "col"))
    total_two, total_three, total_four = sums[0], sums[1], sums[2]

    cube_dense = slab_matmul_nt(s_local, d_far)
    quartic_dense = slab_matmul_nt(s_local, s_far)
    gamma_mix = (target_trace[0] - 4.0 * total_three + 3.0 * total_four) / (
        total_two - 2.0 * total_three + total_four + 1e-06
    )
    carried = pick(
        jnp.pad(s_local, ((0, 0), (0, 0), (HALF, HALF), (0, 0))), update_cols, -3 * HALF
    ).astype(F32)
    cube_part = pick(cube_dense, update_cols, -3 * HALF)
    quartic_part = pick(quartic_dense, update_cols, -3 * HALF)
    purified = (
        (4.0 - 2.0 * gamma_mix) * cube_part
        + (gamma_mix - 3.0) * quartic_part
        + gamma_mix * carried
    ).astype(BF16)
    return (square, purified)


def solution(mesh):
    return jax.shard_map(
        shards,
        mesh=mesh,
        in_specs=(
            P(("row", "col"), None, None, None),
            P(("row", "col"), None),
            P(("row", "col")),
            P(("row", "col"), None),
            P(("row", "col"), None),
            P(),
        ),
        out_specs=(P(("row", "col"), None, None, None), P(("row", "col"), None, None, None)),
        check_vma=False,
    )
```

```python
import jax
import jax.numpy as jnp
from jax import lax
from jax.experimental import pallas as pl
from jax.experimental.pallas import tpu as pltpu
from jax.sharding import PartitionSpec as P

HALF = 4
BF16 = jnp.bfloat16
F32 = jnp.float32


def passed_along(value, axis, steps):
    count = lax.axis_size(axis)
    pairs = [(source, (source + steps) % count) for source in range(count)]
    return lax.ppermute(value, axis, pairs)


def assemble(earlier, own_parts, later):
    joined = []
    for member in range(len(own_parts)):
        pieces = (
            [arrival[member] for arrival in reversed(earlier)]
            + [own_parts[member]]
            + [arrival[member] for arrival in later]
        )
        joined.append(jnp.concatenate(pieces, axis=0))
    return tuple(joined)


def spread(blocks, columns, reach_devices):
    earlier, later = ([], [])
    for heading, arrivals in ((1, earlier), (-1, later)):
        carried = (blocks, columns)
        for _ in range(reach_devices):
            carried = passed_along(carried, ("row", "col"), heading)
            arrivals.append(carried)
    ordered = list(reversed(earlier)) + [(blocks, columns)] + later
    return [part[0] for part in ordered], jnp.concatenate([part[1] for part in ordered], axis=0)


def butterfly_sum(value, axes):
    count = 1
    for axis in axes:
        count *= lax.axis_size(axis)
    step = 1
    while step < count:
        pairs = [(source, source ^ step) for source in range(count)]
        value = value + lax.ppermute(value, axes, pairs)
        step *= 2
    return value


def place_onehot(first_row, row_count, columns, low, width):
    rows = jnp.arange(row_count, dtype=jnp.int32)[:, None, None] + first_row
    target = rows + columns[:, None, :] - low
    places = jnp.arange(width, dtype=jnp.int32)[None, :, None]
    return (target == places).astype(BF16)


def densify(blocks, columns, first_row, low, width):
    onehot = place_onehot(first_row, blocks.shape[0], columns, low, width)
    dense = jnp.einsum("rcs,rsyz->rycz", onehot, blocks, preferred_element_type=F32)
    return dense.astype(BF16)


def densify_transposed(pieces, columns, first_row, low, width, row_range):
    top_row, end_row = row_range
    count = end_row - top_row
    slots, b = pieces[0].shape[1], pieces[0].shape[2]
    columns = columns[top_row:end_row]
    rows = jnp.arange(count, dtype=jnp.int32)[:, None] + first_row
    place = rows + columns - low
    valid = ((place >= 0) & (place < width)).astype(jnp.int32)
    place = jnp.where(valid > 0, place, 0).astype(jnp.int32)
    spans, used, offset = [], [], 0
    for piece in pieces:
        lo, hi = max(offset, top_row), min(offset + piece.shape[0], end_row)
        if lo < hi:
            spans.append((lo - offset, hi - lo, lo - top_row))
            used.append(piece)
        offset += piece.shape[0]

    def kernel(place_ref, valid_ref, *refs):
        out_ref = refs[-1]

        def clear(c, carry):
            start = pl.multiple_of(c * b, b)
            out_ref[pl.ds(start, b), :] = jnp.zeros((b, count * b), out_ref.dtype)
            return carry

        lax.fori_loop(0, width, clear, 0)
        for piece_ref, (skip, take, dest) in zip(refs[:-1], spans):

            def put(i, carry, piece_ref=piece_ref, skip=skip, dest=dest):
                r = i // slots
                s = i % slots

                @pl.when(valid_ref[dest + r, s] > 0)
                def _():
                    top = pl.multiple_of(place_ref[dest + r, s] * b, b)
                    left = pl.multiple_of((dest + r) * b, b)
                    out_ref[pl.ds(top, b), pl.ds(left, b)] = piece_ref[skip + r, s]

                return carry

            lax.fori_loop(0, take * slots, put, 0)

    moved = sum(piece.size for piece in used) * 2 + width * b * count * b * 2
    return pl.pallas_call(
        kernel,
        out_shape=jax.ShapeDtypeStruct((width * b, count * b), BF16),
        in_specs=[pl.BlockSpec(memory_space=pltpu.SMEM)] * 2
        + [pl.BlockSpec(memory_space=pltpu.VMEM)] * len(used),
        out_specs=pl.BlockSpec(memory_space=pltpu.VMEM),
        cost_estimate=pl.CostEstimate(flops=0, bytes_accessed=moved, transcendentals=0),
    )(place, valid, *used)


def slab_matmul_nt(left, right_t):
    r, b, k, _ = left.shape
    n = right_t.shape[0] // b
    out = lax.dot_general(
        left.reshape(r * b, k * b), right_t, (((1,), (1,)), ((), ())), preferred_element_type=F32
    )
    return out.reshape(r, b, n, b)


def slab_matmul(left, right):
    r, b, k, _ = left.shape
    n = right.shape[2]
    out = jnp.dot(
        left.reshape(r * b, k * b), right.reshape(k * b, n * b), preferred_element_type=F32
    )
    return out.reshape(r, b, n, b)


def extract(dense, columns, low):
    onehot = place_onehot(0, dense.shape[0], columns, low, dense.shape[2])
    picked = jnp.einsum("rcs,rxcz->rsxz", onehot, dense, preferred_element_type=F32)
    return picked.astype(BF16)


def pick(dense, columns, low):
    places = jnp.arange(dense.shape[0], dtype=jnp.int32)[:, None] + columns - low
    picked = jnp.take_along_axis(dense, places[:, None, :, None], axis=2)
    return jnp.transpose(picked, (0, 2, 1, 3))


def shards(density_values, density_cols, density_counts, square_cols, update_cols, target_trace):
    rows_here = density_values.shape[0]
    reach_devices = (2 * HALF + rows_here - 1) // rows_here
    margin = reach_devices * rows_here
    is_live = (
        jnp.arange(density_values.shape[1], dtype=jnp.int32)[None, :] < density_counts[:, None]
    )
    masked = jnp.where(is_live[:, :, None, None], density_values, jnp.zeros_like(density_values))
    masked_wide, cols_wide = spread(jnp.swapaxes(masked, 2, 3), density_cols, reach_devices)

    d_local = densify(masked, density_cols, 0, -HALF, rows_here + 2 * HALF)
    near = slice(margin - HALF, margin + rows_here + HALF)
    d_near = densify_transposed(
        masked_wide, cols_wide, -HALF, -2 * HALF, rows_here + 4 * HALF, (near.start, near.stop)
    )
    square_dense = slab_matmul_nt(d_local, d_near).astype(BF16)
    pattern = jnp.max(place_onehot(0, rows_here, square_cols, -2 * HALF, rows_here + 4 * HALF), axis=2)
    s_local = jnp.where(pattern[:, None, :, None] > 0, square_dense, jnp.zeros_like(square_dense))
    square = extract(s_local, square_cols, -2 * HALF)

    square_wide, square_cols_wide = spread(jnp.swapaxes(square, 2, 3), square_cols, reach_devices)
    far = slice(margin - 2 * HALF, margin + rows_here + 2 * HALF)
    d_far = densify_transposed(
        masked_wide, cols_wide, -2 * HALF, -3 * HALF, rows_here + 6 * HALF, (far.start, far.stop)
    )
    s_far = densify_transposed(
        square_wide,
        square_cols_wide,
        -2 * HALF,
        -3 * HALF,
        rows_here + 6 * HALF,
        (far.start, far.stop),
    )

    trace_two = jnp.sum(jnp.square(masked.astype(F32)))
    trace_three = jnp.sum(
        s_local[:, :, HALF : HALF + rows_here + 2 * HALF, :].astype(F32) * d_local.astype(F32)
    )
    trace_four = jnp.sum(jnp.square(s_local.astype(F32)))
    local_sums, _, _ = lax.optimization_barrier(
        (jnp.stack([trace_two, trace_three, trace_four]), square_wide[0], square_wide[-1])
    )
    sums = butterfly_sum(local_sums, ("row", "col"))
    total_two, total_three, total_four = sums[0], sums[1], sums[2]

    cube_dense = slab_matmul_nt(s_local, d_far)
    quartic_dense = slab_matmul_nt(s_local, s_far)
    gamma_mix = (target_trace[0] - 4.0 * total_three + 3.0 * total_four) / (
        total_two - 2.0 * total_three + total_four + 1e-06
    )
    carried = pick(
        jnp.pad(s_local, ((0, 0), (0, 0), (HALF, HALF), (0, 0))), update_cols, -3 * HALF
    ).astype(F32)
    cube_part = pick(cube_dense, update_cols, -3 * HALF)
    quartic_part = pick(quartic_dense, update_cols, -3 * HALF)
    purified = (
        (4.0 - 2.0 * gamma_mix) * cube_part
        + (gamma_mix - 3.0) * quartic_part
        + gamma_mix * carried
    ).astype(BF16)
    return (square, purified)


def solution(mesh):
    return jax.shard_map(
        shards,
        mesh=mesh,
        in_specs=(
            P(("row", "col"), None, None, None),
            P(("row", "col"), None),
            P(("row", "col")),
            P(("row", "col"), None),
            P(("row", "col"), None),
            P(),
        ),
        out_specs=(P(("row", "col"), None, None, None), P(("row", "col"), None, None, None)),
        check_vma=False,
    )
```

```python
import jax
import jax.numpy as jnp
from jax import lax
from jax.experimental import pallas as pl
from jax.experimental.pallas import tpu as pltpu
from jax.sharding import PartitionSpec as P

HALF = 4
BF16 = jnp.bfloat16
F32 = jnp.float32


def passed_along(value, axis, steps):
    count = lax.axis_size(axis)
    pairs = [(source, (source + steps) % count) for source in range(count)]
    return lax.ppermute(value, axis, pairs)


def assemble(earlier, own_parts, later):
    joined = []
    for member in range(len(own_parts)):
        pieces = (
            [arrival[member] for arrival in reversed(earlier)]
            + [own_parts[member]]
            + [arrival[member] for arrival in later]
        )
        joined.append(jnp.concatenate(pieces, axis=0))
    return tuple(joined)


def spread(blocks, columns, reach_devices):
    count, slots, b, _ = blocks.shape
    tag = jnp.pad(
        columns.astype(BF16)[:, None, None, :], ((0, 0), (0, 0), (0, b - 1), (0, b - slots))
    )
    payload = jnp.concatenate([blocks, tag], axis=1)
    earlier, later = ([], [])
    for heading, arrivals in ((1, earlier), (-1, later)):
        carried = payload
        for _ in range(reach_devices):
            carried = passed_along(carried, ("row", "col"), heading)
            arrivals.append(carried)
    pieces = list(reversed(earlier)) + [payload] + later
    joined = [piece[:, slots, 0, :slots].astype(jnp.int32) for piece in reversed(earlier)]
    joined += [columns] + [piece[:, slots, 0, :slots].astype(jnp.int32) for piece in later]
    return pieces, jnp.concatenate(joined, axis=0)


def butterfly_sum(value, axes):
    count = 1
    for axis in axes:
        count *= lax.axis_size(axis)
    step = 1
    while step < count:
        pairs = [(source, source ^ step) for source in range(count)]
        value = value + lax.ppermute(value, axes, pairs)
        step *= 2
    return value


def place_onehot(first_row, row_count, columns, low, width):
    rows = jnp.arange(row_count, dtype=jnp.int32)[:, None, None] + first_row
    target = rows + columns[:, None, :] - low
    places = jnp.arange(width, dtype=jnp.int32)[None, :, None]
    return (target == places).astype(BF16)


def densify(blocks, columns, first_row, low, width):
    onehot = place_onehot(first_row, blocks.shape[0], columns, low, width)
    dense = jnp.einsum("rcs,rsyz->rycz", onehot, blocks, preferred_element_type=F32)
    return dense.astype(BF16)


def densify_transposed(pieces, columns, first_row, low, width, row_range):
    top_row, end_row = row_range
    count = end_row - top_row
    slots, b = columns.shape[1], pieces[0].shape[2]
    columns = columns[top_row:end_row]
    rows = jnp.arange(count, dtype=jnp.int32)[:, None] + first_row
    place = rows + columns - low
    valid = ((place >= 0) & (place < width)).astype(jnp.int32)
    place = jnp.where(valid > 0, place, 0).astype(jnp.int32)
    spans, used, offset = [], [], 0
    for piece in pieces:
        lo, hi = max(offset, top_row), min(offset + piece.shape[0], end_row)
        if lo < hi:
            spans.append((lo - offset, hi - lo, lo - top_row))
            used.append(piece)
        offset += piece.shape[0]

    def kernel(place_ref, valid_ref, *refs):
        out_ref = refs[-1]

        def clear(c, carry):
            start = pl.multiple_of(c * b, b)
            out_ref[pl.ds(start, b), :] = jnp.zeros((b, count * b), out_ref.dtype)
            return carry

        lax.fori_loop(0, width, clear, 0)
        for piece_ref, (skip, take, dest) in zip(refs[:-1], spans):

            def put(i, carry, piece_ref=piece_ref, skip=skip, dest=dest):
                r = i // slots
                s = i % slots

                @pl.when(valid_ref[dest + r, s] > 0)
                def _():
                    top = pl.multiple_of(place_ref[dest + r, s] * b, b)
                    left = pl.multiple_of((dest + r) * b, b)
                    out_ref[pl.ds(top, b), pl.ds(left, b)] = piece_ref[skip + r, s]

                return carry

            lax.fori_loop(0, take * slots, put, 0)

    moved = sum(piece.size for piece in used) * 2 + width * b * count * b * 2
    return pl.pallas_call(
        kernel,
        out_shape=jax.ShapeDtypeStruct((width * b, count * b), BF16),
        in_specs=[pl.BlockSpec(memory_space=pltpu.SMEM)] * 2
        + [pl.BlockSpec(memory_space=pltpu.VMEM)] * len(used),
        out_specs=pl.BlockSpec(memory_space=pltpu.VMEM),
        cost_estimate=pl.CostEstimate(flops=0, bytes_accessed=moved, transcendentals=0),
    )(place, valid, *used)


def slab_matmul_nt(left, right_t):
    r, b, k, _ = left.shape
    n = right_t.shape[0] // b
    out = lax.dot_general(
        left.reshape(r * b, k * b), right_t, (((1,), (1,)), ((), ())), preferred_element_type=F32
    )
    return out.reshape(r, b, n, b)


def slab_matmul(left, right):
    r, b, k, _ = left.shape
    n = right.shape[2]
    out = jnp.dot(
        left.reshape(r * b, k * b), right.reshape(k * b, n * b), preferred_element_type=F32
    )
    return out.reshape(r, b, n, b)


def extract(dense, columns, low):
    onehot = place_onehot(0, dense.shape[0], columns, low, dense.shape[2])
    picked = jnp.einsum("rcs,rxcz->rsxz", onehot, dense, preferred_element_type=F32)
    return picked.astype(BF16)


def pick(dense, columns, low):
    places = jnp.arange(dense.shape[0], dtype=jnp.int32)[:, None] + columns - low
    picked = jnp.take_along_axis(dense, places[:, None, :, None], axis=2)
    return jnp.transpose(picked, (0, 2, 1, 3))


def shards(density_values, density_cols, density_counts, square_cols, update_cols, target_trace):
    rows_here = density_values.shape[0]
    reach_devices = (2 * HALF + rows_here - 1) // rows_here
    margin = reach_devices * rows_here
    is_live = (
        jnp.arange(density_values.shape[1], dtype=jnp.int32)[None, :] < density_counts[:, None]
    )
    masked = jnp.where(is_live[:, :, None, None], density_values, jnp.zeros_like(density_values))
    masked_wide, cols_wide = spread(jnp.swapaxes(masked, 2, 3), density_cols, reach_devices)

    d_local = densify(masked, density_cols, 0, -HALF, rows_here + 2 * HALF)
    near = slice(margin - HALF, margin + rows_here + HALF)
    d_near = densify_transposed(
        masked_wide, cols_wide, -HALF, -2 * HALF, rows_here + 4 * HALF, (near.start, near.stop)
    )
    square_dense = slab_matmul_nt(d_local, d_near).astype(BF16)
    pattern = jnp.max(place_onehot(0, rows_here, square_cols, -2 * HALF, rows_here + 4 * HALF), axis=2)
    s_local = jnp.where(pattern[:, None, :, None] > 0, square_dense, jnp.zeros_like(square_dense))
    square = extract(s_local, square_cols, -2 * HALF)

    square_wide, square_cols_wide = spread(jnp.swapaxes(square, 2, 3), square_cols, reach_devices)
    far = slice(margin - 2 * HALF, margin + rows_here + 2 * HALF)
    d_far = densify_transposed(
        masked_wide, cols_wide, -2 * HALF, -3 * HALF, rows_here + 6 * HALF, (far.start, far.stop)
    )
    s_far = densify_transposed(
        square_wide,
        square_cols_wide,
        -2 * HALF,
        -3 * HALF,
        rows_here + 6 * HALF,
        (far.start, far.stop),
    )

    trace_two = jnp.sum(jnp.square(masked.astype(F32)))
    trace_three = jnp.sum(
        s_local[:, :, HALF : HALF + rows_here + 2 * HALF, :].astype(F32) * d_local.astype(F32)
    )
    trace_four = jnp.sum(jnp.square(s_local.astype(F32)))
    local_sums, _, _ = lax.optimization_barrier(
        (jnp.stack([trace_two, trace_three, trace_four]), square_wide[0], square_wide[-1])
    )
    sums = butterfly_sum(local_sums, ("row", "col"))
    total_two, total_three, total_four = sums[0], sums[1], sums[2]

    cube_dense = slab_matmul_nt(s_local, d_far)
    quartic_dense = slab_matmul_nt(s_local, s_far)
    gamma_mix = (target_trace[0] - 4.0 * total_three + 3.0 * total_four) / (
        total_two - 2.0 * total_three + total_four + 1e-06
    )
    carried = pick(
        jnp.pad(s_local, ((0, 0), (0, 0), (HALF, HALF), (0, 0))), update_cols, -3 * HALF
    ).astype(F32)
    cube_part = pick(cube_dense, update_cols, -3 * HALF)
    quartic_part = pick(quartic_dense, update_cols, -3 * HALF)
    purified = (
        (4.0 - 2.0 * gamma_mix) * cube_part
        + (gamma_mix - 3.0) * quartic_part
        + gamma_mix * carried
    ).astype(BF16)
    return (square, purified)


def solution(mesh):
    return jax.shard_map(
        shards,
        mesh=mesh,
        in_specs=(
            P(("row", "col"), None, None, None),
            P(("row", "col"), None),
            P(("row", "col")),
            P(("row", "col"), None),
            P(("row", "col"), None),
            P(),
        ),
        out_specs=(P(("row", "col"), None, None, None), P(("row", "col"), None, None, None)),
        check_vma=False,
    )
```

```python
import jax
import jax.numpy as jnp
from jax import lax
from jax.experimental import pallas as pl
from jax.experimental.pallas import tpu as pltpu
from jax.sharding import PartitionSpec as P

HALF = 4
QUARTERS = 4
BF16 = jnp.bfloat16
F32 = jnp.float32


def passed_along(value, axis, steps):
    count = lax.axis_size(axis)
    pairs = [(source, (source + steps) % count) for source in range(count)]
    return lax.ppermute(value, axis, pairs)


def spread(blocks, columns, reach_devices):
    earlier, later = ([], [])
    for heading, arrivals in ((1, earlier), (-1, later)):
        carried = (blocks, columns)
        for _ in range(reach_devices):
            carried = passed_along(carried, ("row", "col"), heading)
            arrivals.append(carried)
    ordered = list(reversed(earlier)) + [(blocks, columns)] + later
    return [part[0] for part in ordered], jnp.concatenate([part[1] for part in ordered], axis=0)


def butterfly_sum(value, axes):
    count = 1
    for axis in axes:
        count *= lax.axis_size(axis)
    step, round_index = 1, 0
    while step < count:
        pairs = [(source, source ^ step) for source in range(count)]
        value = value + lax.ppermute(value, axes, pairs)
        step *= 2
        round_index += 1
    return value


def place_onehot(first_row, row_count, columns, low, width):
    rows = jnp.arange(row_count, dtype=jnp.int32)[:, None, None] + first_row
    target = rows + columns[:, None, :] - low
    places = jnp.arange(width, dtype=jnp.int32)[None, :, None]
    return (target == places).astype(BF16)


def densify(blocks, columns, first_row, low, width):
    onehot = place_onehot(first_row, blocks.shape[0], columns, low, width)
    dense = jnp.einsum("rcs,rsyz->rycz", onehot, blocks, preferred_element_type=F32)
    return dense.astype(BF16)


def densify_transposed(pieces, columns, first_row, low, width, row_range):
    top_row, end_row = row_range
    count = end_row - top_row
    slots, b = pieces[0].shape[1], pieces[0].shape[2]
    columns = columns[top_row:end_row]
    rows = jnp.arange(count, dtype=jnp.int32)[:, None] + first_row
    place = rows + columns - low
    valid = ((place >= 0) & (place < width)).astype(jnp.int32)
    place = jnp.where(valid > 0, place, 0).astype(jnp.int32)
    spans, used, offset = [], [], 0
    for piece in pieces:
        lo, hi = max(offset, top_row), min(offset + piece.shape[0], end_row)
        if lo < hi:
            spans.append((lo - offset, hi - lo, lo - top_row))
            used.append(piece)
        offset += piece.shape[0]

    def kernel(place_ref, valid_ref, *refs):
        out_ref = refs[-1]

        def clear(c, carry):
            start = pl.multiple_of(c * b, b)
            out_ref[pl.ds(start, b), :] = jnp.zeros((b, count * b), out_ref.dtype)
            return carry

        lax.fori_loop(0, width, clear, 0)
        for piece_ref, (skip, take, dest) in zip(refs[:-1], spans):

            def put(i, carry, piece_ref=piece_ref, skip=skip, dest=dest):
                r = i // slots
                s = i % slots

                @pl.when(valid_ref[dest + r, s] > 0)
                def _():
                    top = pl.multiple_of(place_ref[dest + r, s] * b, b)
                    left = pl.multiple_of((dest + r) * b, b)
                    out_ref[pl.ds(top, b), pl.ds(left, b)] = piece_ref[skip + r, s]

                return carry

            lax.fori_loop(0, take * slots, put, 0)

    moved = sum(piece.size for piece in used) * 2 + width * b * count * b * 2
    return pl.pallas_call(
        kernel,
        out_shape=jax.ShapeDtypeStruct((width * b, count * b), BF16),
        in_specs=[pl.BlockSpec(memory_space=pltpu.SMEM)] * 2
        + [pl.BlockSpec(memory_space=pltpu.VMEM)] * len(used),
        out_specs=pl.BlockSpec(memory_space=pltpu.VMEM),
        cost_estimate=pl.CostEstimate(flops=0, bytes_accessed=moved, transcendentals=0),
    )(place, valid, *used)


def slab_matmul_nt(left, right_t):
    r, b, k, _ = left.shape
    n = right_t.shape[0] // b
    out = lax.dot_general(
        left.reshape(r * b, k * b), right_t, (((1,), (1,)), ((), ())), preferred_element_type=F32
    )
    return out.reshape(r, b, n, b)


def extract(dense, columns, low):
    onehot = place_onehot(0, dense.shape[0], columns, low, dense.shape[2])
    picked = jnp.einsum("rcs,rxcz->rsxz", onehot, dense, preferred_element_type=F32)
    return picked.astype(BF16)


def pick(dense, columns, low):
    places = jnp.arange(dense.shape[0], dtype=jnp.int32)[:, None] + columns - low
    picked = jnp.take_along_axis(dense, places[:, None, :, None], axis=2)
    return jnp.transpose(picked, (0, 2, 1, 3))


def shards(density_values, density_cols, density_counts, square_cols, update_cols, target_trace):
    rows_here = density_values.shape[0]
    reach_devices = (2 * HALF + rows_here - 1) // rows_here
    margin = reach_devices * rows_here
    is_live = (
        jnp.arange(density_values.shape[1], dtype=jnp.int32)[None, :] < density_counts[:, None]
    )
    masked = jnp.where(is_live[:, :, None, None], density_values, jnp.zeros_like(density_values))
    masked_wide, cols_wide = spread(jnp.swapaxes(masked, 2, 3), density_cols, reach_devices)

    d_local = densify(masked, density_cols, 0, -HALF, rows_here + 2 * HALF)
    near = slice(margin - HALF, margin + rows_here + HALF)
    d_near = densify_transposed(
        masked_wide, cols_wide, -HALF, -2 * HALF, rows_here + 4 * HALF, (near.start, near.stop)
    )
    square_dense = slab_matmul_nt(d_local, d_near).astype(BF16)
    pattern = jnp.max(place_onehot(0, rows_here, square_cols, -2 * HALF, rows_here + 4 * HALF), axis=2)
    s_local = jnp.where(pattern[:, None, :, None] > 0, square_dense, jnp.zeros_like(square_dense))
    square = extract(s_local, square_cols, -2 * HALF)

    square_wide, square_cols_wide = spread(jnp.swapaxes(square, 2, 3), square_cols, reach_devices)
    far = slice(margin - 2 * HALF, margin + rows_here + 2 * HALF)
    d_far = densify_transposed(
        masked_wide, cols_wide, -2 * HALF, -3 * HALF, rows_here + 6 * HALF, (far.start, far.stop)
    )
    s_far = densify_transposed(
        square_wide,
        square_cols_wide,
        -2 * HALF,
        -3 * HALF,
        rows_here + 6 * HALF,
        (far.start, far.stop),
    )

    trace_two = jnp.sum(jnp.square(masked.astype(F32)))
    trace_three = jnp.sum(
        s_local[:, :, HALF : HALF + rows_here + 2 * HALF, :].astype(F32) * d_local.astype(F32)
    )
    trace_four = jnp.sum(jnp.square(s_local.astype(F32)))
    local_sums, _, _ = lax.optimization_barrier(
        (jnp.stack([trace_two, trace_three, trace_four]), square_wide[0], square_wide[-1])
    )
    sums = butterfly_sum(local_sums, ("row", "col"))
    total_two, total_three, total_four = sums[0], sums[1], sums[2]

    cube_dense = slab_matmul_nt(s_local, d_far)
    block = s_local.shape[1]
    width_cols = s_far.shape[0] // block
    quarters = QUARTERS if width_cols % QUARTERS == 0 else 1
    per = width_cols // quarters
    places = jnp.arange(rows_here, dtype=jnp.int32)[:, None] + update_cols + 3 * HALF
    quartic_part = None
    for q in range(quarters):
        dense_q = slab_matmul_nt(s_local, s_far[q * per * block : (q + 1) * per * block])
        local = jnp.clip(places - q * per, 0, per - 1)
        got = jnp.transpose(
            jnp.take_along_axis(dense_q, local[:, None, :, None], axis=2), (0, 2, 1, 3)
        )
        inside = (places >= q * per) & (places < (q + 1) * per)
        quartic_part = got if quartic_part is None else jnp.where(inside[:, :, None, None], got, quartic_part)
    gamma_mix = (target_trace[0] - 4.0 * total_three + 3.0 * total_four) / (
        total_two - 2.0 * total_three + total_four + 1e-06
    )
    carried = pick(
        jnp.pad(s_local, ((0, 0), (0, 0), (HALF, HALF), (0, 0))), update_cols, -3 * HALF
    ).astype(F32)
    cube_part = pick(cube_dense, update_cols, -3 * HALF)
    purified = (
        (4.0 - 2.0 * gamma_mix) * cube_part
        + (gamma_mix - 3.0) * quartic_part
        + gamma_mix * carried
    ).astype(BF16)
    return (square, purified)


def solution(mesh):
    return _mapped(mesh)


def _mapped(mesh):
    return jax.shard_map(
        shards,
        mesh=mesh,
        in_specs=(
            P(("row", "col"), None, None, None),
            P(("row", "col"), None),
            P(("row", "col")),
            P(("row", "col"), None),
            P(("row", "col"), None),
            P(),
        ),
        out_specs=(P(("row", "col"), None, None, None), P(("row", "col"), None, None, None)),
        check_vma=False,
    )
```
